128 devices in a mesh: sec: 2 (over y_hi), seq: 8 (over x, core), trk: 8 (over y_lo, z).
Axes of the slice: x: 4, y: 4 (y_hi: 2, y_lo: 2; y = y_hi * 2 + y_lo), z: 4, core: 2. Of those that a mesh axis runs over, the one named last changes fastest.
Arguments:
- tokens: bfloat16 [8, 512, 1536], P('sec', 'seq'), may hold values from -6 to 6
- norm_gain: bfloat16 [1536], replicated, may hold values from 0.25 to 1.75
- dilated_conv_weight: bfloat16 [1536, 3, 1536], P(None, None, 'trk'), may hold values from -0.09375 to 0.09375
- head_weight: bfloat16 [1536, 8, 20, 128], P(None, 'trk'), may hold values from -0.15625 to 0.15625
- targets: bfloat16 [8, 512, 8, 20, 128], P('sec', 'seq', 'trk'), may hold values from 0 to 2
- owner_tiles: int32 [8, 20], P('trk'), may hold values from -1 to 80, as said below
- species: int32 [8], P('sec'), may hold values from 0 to 1, as said below
Outputs:
- conv_grad: float32 [1536, 3, 1536], P(('sec', 'seq'), None, 'trk')
- head_grad: float32 [1536, 8, 20, 128], P(('sec', 'seq'), 'trk')
The draws below stay inside these ranges and needn't reach their ends.
Inputs may be any that keep to these rules, and one draw needn't show every extreme that they name: `owner_tiles`: each of the 81 tiles (human tiles 0 to 59, then the mouse tiles) stands in exactly one slot of one owner; -1 marks an empty slot; in every draw one owner has all 20 slots filled. `species`: 0 is human, 1 is mouse; exactly half of the samples are mouse.
All inputs are finite; a program needn't handle non-finite values.
Results may differ from the reference program's by a relative error of at most 0.0023.
Values may be sent and summed in bfloat16 or wider, within the bound.
No kernel may reach another device: no remote copies, remote signals or barrier semaphores. Data moves between devices by JAX's collectives and lax.ppermute only.
A program may use at most 128 MiB of HBM per device.

```python
import math
import jax
import jax.numpy as jnp
from jax import lax

C = 1536
HTRACKS = 7611
MTRACKS = 2608
DILATION_BINS = 16
TAPS = 3
HTILES = 60
TILES = 81
SLOTS = 20
OWNERS = 8
SAMPLES = 8
SEQUENCE_BINS = 512
N_TRK = 8


def draw_owner_tiles(key, part):
    key_perm = jax.random.fold_in(key, 11)
    key_full = jax.random.fold_in(key, 12)
    key_place = jax.random.fold_in(key, 13)
    tile_order = jax.random.permutation(key_perm, TILES).astype(jnp.int32)
    full_owner = jax.random.randint(key_full, (), 0, N_TRK).astype(jnp.int32)
    other_slots = (N_TRK - 1) * SLOTS
    placing = jax.random.permutation(key_place, max(other_slots, 1)).astype(jnp.int32)
    others = jnp.full((max(other_slots, 1),), -1, jnp.int32)
    others = others.at[placing[:TILES - SLOTS]].set(tile_order[SLOTS:])
    others = others[:other_slots].reshape(N_TRK - 1, SLOTS)
    owner_rows = jnp.arange(N_TRK, dtype=jnp.int32)
    other_index = jnp.clip(jnp.where(owner_rows < full_owner, owner_rows, owner_rows - 1), 0, max(N_TRK - 2, 0))
    picked = jnp.take(others, other_index, axis=0)
    return jnp.where((owner_rows == full_owner)[:, None], tile_order[:SLOTS][None, :], picked).astype(jnp.int32)


def draw_species(key, part):
    order = jax.random.permutation(jax.random.fold_in(key, 21), SAMPLES).astype(jnp.int32)
    return (order % 2).astype(jnp.int32)


def level_of(stream_key, extent, split, least, top_value):
    factor_of = 1.0
    for dim, parts in split:
        draws = jax.random.uniform(jax.random.fold_in(jax.random.fold_in(stream_key, 6), dim), (parts,), jnp.float32, least / len(split), top_value / len(split))
        factor_of = factor_of * jnp.repeat(jnp.exp(draws), extent[dim] // parts).reshape((-1,) + (1,) * (len(extent) - 1 - dim))
    return factor_of


def centred(stream_key, extent, scale, bound, cuts=(), kind=jnp.bfloat16):
    array = scale * jax.random.normal(stream_key, extent, jnp.float32)
    if cuts:
        array = array * level_of(stream_key, extent, cuts, -0.22, 0.18)
    return jnp.clip(array, -bound, bound).astype(kind)


def setup_inputs(seed: int = 0) -> dict:
    streams_of = jax.random.split(jax.random.key(seed), 8)
    return {
        "tokens": centred(streams_of[0], (SAMPLES, SEQUENCE_BINS, C), 1.0, 6.0, ((0, 2), (1, 8))),
        "norm_gain": jnp.clip(1.0 + 0.15 * jax.random.normal(streams_of[1], (C,), jnp.float32), 0.25, 1.75).astype(jnp.bfloat16),
        "dilated_conv_weight": centred(streams_of[2], (C, TAPS, C), (TAPS * C) ** -0.5, 0.09375, ((2, 8),)),
        "head_weight": centred(streams_of[3], (C, OWNERS, SLOTS, 128), C ** -0.5, 0.15625, ((1, 8),)),
        "targets": jnp.clip(2.0 * jax.random.uniform(streams_of[4], (SAMPLES, SEQUENCE_BINS, OWNERS, SLOTS, 128), jnp.float32) ** level_of(streams_of[4], (SAMPLES, SEQUENCE_BINS, OWNERS, SLOTS, 128), ((0, 2), (1, 8), (2, 8)), -0.2, 0.2), 0.0, 2.0).astype(jnp.bfloat16),
        "owner_tiles": draw_owner_tiles(jax.random.fold_in(streams_of[7], 71), 0),
        "species": draw_species(jax.random.fold_in(streams_of[7], 71), 0),
    }


def contracted_rows(left, right):
    return lax.dot_general(left, right, (((0,), (0,)), ((), ())), preferred_element_type=jnp.float32)

def reference(tokens, norm_gain, dilated_conv_weight, head_weight, targets, owner_tiles, species):
    inputs = tokens.astype(jnp.float32)
    mean_sq = lax.optimization_barrier(jnp.mean(inputs * inputs, axis=-1, keepdims=True))
    normed = inputs * lax.rsqrt(mean_sq + 1e-06) * norm_gain.astype(jnp.float32)
    hidden_state = jax.nn.gelu(normed).astype(jnp.bfloat16)
    padded_input = jnp.pad(hidden_state, ((0, 0), (DILATION_BINS, DILATION_BINS), (0, 0)))
    tap_count = dilated_conv_weight.shape[1]
    mixed_list = []
    for sample_input in range(SAMPLES):
        convolution_output = jnp.zeros((SEQUENCE_BINS, C), jnp.float32)
        for kernel_tap_index in range(tap_count):
            convolution_output = convolution_output + jnp.dot(padded_input[sample_input, kernel_tap_index * DILATION_BINS:kernel_tap_index * DILATION_BINS + SEQUENCE_BINS], dilated_conv_weight[:, kernel_tap_index, :], preferred_element_type=jnp.float32)
        mixed_list.append((inputs[sample_input] + convolution_output).astype(jnp.bfloat16))
    mixed_all = jnp.stack(mixed_list)
    grad_scale = 1.0 / math.sqrt(SAMPLES * SEQUENCE_BINS)
    lane_ids = jnp.arange(128, dtype=jnp.int32)

    def owner_step(back_sum, owner_index):
        weights_owner = lax.dynamic_index_in_dim(head_weight, owner_index, 1, keepdims=False)
        tiles_owner = lax.dynamic_index_in_dim(owner_tiles, owner_index, 0, keepdims=False).astype(jnp.int32)
        targets_owner = lax.dynamic_index_in_dim(targets, owner_index, 2, keepdims=False)
        is_mouse = tiles_owner >= HTILES
        within = jnp.where(is_mouse, tiles_owner - HTILES, tiles_owner)
        track_limit = jnp.where(is_mouse, MTRACKS, HTRACKS).astype(jnp.int32)
        lane_mask = (within[:, None] * 128 + lane_ids[None, :] < track_limit[:, None]).astype(jnp.float32)
        grads_owner = jnp.zeros((C, SLOTS, 128), jnp.float32)
        new_back = []
        for sample_input in range(SAMPLES):
            active_int = ((tiles_owner >= 0) & (is_mouse == (species[sample_input] == 1))).astype(jnp.int32)
            slot_order = jnp.argsort(1 - active_int, stable=True).astype(jnp.int32)
            live_count = jnp.sum(active_int).astype(jnp.int32)
            mixed_here = mixed_all[sample_input]
            target_here = targets_owner[sample_input]

            def slot_step(position, loop_state):
                grads_now, back_now = loop_state
                slot_index = slot_order[position]
                column_w = lax.dynamic_index_in_dim(weights_owner, slot_index, 1, keepdims=False)
                logits = jnp.dot(mixed_here, column_w, preferred_element_type=jnp.float32)
                target_cols = lax.dynamic_index_in_dim(target_here, slot_index, 1, keepdims=False).astype(jnp.float32)
                mask_row = lax.dynamic_index_in_dim(lane_mask, slot_index, 0, keepdims=False)
                delta_f = grad_scale * (jax.nn.softplus(logits) - target_cols) * jax.nn.sigmoid(logits) * mask_row[None, :]
                delta_b = delta_f.astype(jnp.bfloat16)
                grads_now = grads_now.at[:, slot_index, :].add(contracted_rows(mixed_here, delta_b))
                back_now = back_now + lax.dot_general(delta_b, column_w, (((1,), (1,)), ((), ())), preferred_element_type=jnp.float32)
                return (grads_now, back_now)
            grads_owner, back_sample = lax.fori_loop(0, live_count, slot_step, (grads_owner, back_sum[sample_input]))
            new_back.append(back_sample)
        return (jnp.stack(new_back), grads_owner)
    back_sum, grads_all = lax.scan(owner_step, jnp.zeros((SAMPLES, SEQUENCE_BINS, C), jnp.float32), jnp.arange(OWNERS, dtype=jnp.int32))
    backward_bias = back_sum.astype(jnp.bfloat16)
    per_tap = []
    for kernel_tap_index in range(tap_count):
        running_total = jnp.zeros((C, C), jnp.float32)
        for sample_input in range(SAMPLES):
            running_total = running_total + contracted_rows(padded_input[sample_input, kernel_tap_index * DILATION_BINS:kernel_tap_index * DILATION_BINS + SEQUENCE_BINS], backward_bias[sample_input])
        per_tap.append(running_total)
    conv_grad = jnp.stack(per_tap, axis=1)
    total_sq = jnp.sum(grads_all * grads_all)
    entries = C * OWNERS * SLOTS * 128
    factor = jnp.minimum(1.0, 0.1 * lax.rsqrt(total_sq / entries + 1e-06))
    head_grad = jnp.transpose(grads_all * factor, (1, 0, 2, 3))
    return (conv_grad, head_grad)
```

```python
import math

import jax
import jax.numpy as jnp
from jax import lax
from jax.sharding import PartitionSpec as P

HTRACKS = 7611
MTRACKS = 2608
DILATION_BINS = 16
HTILES = 60


grad_clip = 0.1


def padded(cells, sides, width):
    for axis, dim in sides:
        count = lax.axis_size(axis)
        ends = count - 1
        head = lax.slice_in_dim(cells, 0, width, axis=dim)
        tail = lax.slice_in_dim(cells, cells.shape[dim] - width, cells.shape[dim], axis=dim)
        cells = jnp.concatenate(
            [
                lax.ppermute(tail, axis, [(i, (i + 1) % count) for i in range(ends)]),
                cells,
                lax.ppermute(head, axis, [((i + 1) % count, i) for i in range(ends)]),
            ],
            axis=dim,
        )
    return cells


def contracted_rows(left, right):
    return lax.dot_general(
        left, right, (((0,), (0,)), ((), ())), preferred_element_type=jnp.float32
    )


def body(tokens, norm_gain, dilated_conv_weight, head_weight, targets, owner_tiles, species):
    sample_count = tokens.shape[0]
    local_rows = tokens.shape[1]
    width_all = tokens.shape[2]
    tap_count = dilated_conv_weight.shape[1]
    out_share = dilated_conv_weight.shape[2]
    slot_count = head_weight.shape[2]
    lane_count = head_weight.shape[3]
    inputs = tokens.astype(jnp.float32)
    mean_sq = jnp.mean(inputs * inputs, axis=-1, keepdims=True)
    normed = inputs * lax.rsqrt(mean_sq + 1e-06) * norm_gain.astype(jnp.float32)
    hidden_state = jax.nn.gelu(normed).astype(jnp.bfloat16)
    padded_input = padded(hidden_state, (("seq", 1),), DILATION_BINS)
    convolution_output = jnp.zeros((sample_count, local_rows, out_share), jnp.float32)
    for kernel_tap_index in range(tap_count):
        convolution_output = convolution_output + jnp.dot(
            padded_input[
                :, kernel_tap_index * DILATION_BINS : kernel_tap_index * DILATION_BINS + local_rows
            ],
            dilated_conv_weight[:, kernel_tap_index, :],
            preferred_element_type=jnp.float32,
        )
    own_cols = lax.dynamic_slice_in_dim(inputs, lax.axis_index("trk") * out_share, out_share, 2)
    mixed_share = (own_cols + convolution_output).astype(jnp.bfloat16)
    mixed_all = lax.all_gather(mixed_share, "trk", axis=2, tiled=True)
    tiles_here = owner_tiles[0]
    is_mouse = tiles_here >= HTILES
    within = jnp.where(is_mouse, tiles_here - HTILES, tiles_here)
    track_limit = jnp.where(is_mouse, MTRACKS, HTRACKS).astype(jnp.int32)
    lane_ids = jnp.arange(lane_count, dtype=jnp.int32)
    lane_mask = (within[:, None] * lane_count + lane_ids[None, :] < track_limit[:, None]).astype(
        jnp.float32
    )
    grad_scale = 1.0 / math.sqrt(
        lax.axis_size("sec") * sample_count * lax.axis_size("seq") * local_rows
    )
    weights_here = head_weight[:, 0].reshape(width_all, slot_count * lane_count)
    flat_mixed = mixed_all.reshape(sample_count * local_rows, width_all)
    logits = jnp.dot(flat_mixed, weights_here, preferred_element_type=jnp.float32)
    target_cols = targets[:, :, 0].reshape(sample_count * local_rows, slot_count * lane_count)
    active = (tiles_here[None, :] >= 0) & (is_mouse[None, :] == (species[:, None] == 1))
    live_mask = active.astype(jnp.float32)[:, :, None] * lane_mask[None, :, :]
    live_rows = jnp.broadcast_to(
        live_mask.reshape(sample_count, 1, slot_count * lane_count),
        (sample_count, local_rows, slot_count * lane_count),
    ).reshape(sample_count * local_rows, slot_count * lane_count)
    delta_f = (
        grad_scale
        * (jax.nn.softplus(logits) - target_cols.astype(jnp.float32))
        * jax.nn.sigmoid(logits)
        * live_rows
    )
    flat_deltas = delta_f.astype(jnp.bfloat16)
    back_sum = lax.dot_general(
        flat_deltas, weights_here, (((1,), (1,)), ((), ())), preferred_element_type=jnp.float32
    ).reshape(sample_count, local_rows, width_all)
    backward_portion = lax.psum_scatter(back_sum, "trk", scatter_dimension=2, tiled=True).astype(
        jnp.bfloat16
    )
    group_count = lax.axis_size("sec") * lax.axis_size("seq")
    share_rows = width_all // group_count
    per_tap = [
        lax.dot_general(
            padded_input[
                :, kernel_tap_index * DILATION_BINS : kernel_tap_index * DILATION_BINS + local_rows
            ],
            backward_portion,
            (((0, 1), (0, 1)), ((), ())),
            preferred_element_type=jnp.float32,
        )
        for kernel_tap_index in range(tap_count)
    ]
    conv_grad = lax.psum_scatter(
        jnp.stack(per_tap, axis=1), ("sec", "seq"), scatter_dimension=0, tiled=True
    )
    grad_share = lax.psum_scatter(
        contracted_rows(flat_mixed, flat_deltas), ("sec", "seq"), scatter_dimension=0, tiled=True
    )
    total_sq = lax.psum(jnp.sum(grad_share * grad_share), ("sec", "seq", "trk"))
    entries = width_all * lax.axis_size("trk") * slot_count * lane_count
    factor = jnp.minimum(1.0, grad_clip * lax.rsqrt(total_sq / entries + 1e-06))
    head_grad = (grad_share * factor).reshape(share_rows, 1, slot_count, lane_count)
    return (conv_grad, head_grad)


def solution(mesh):
    return jax.shard_map(
        body,
        mesh=mesh,
        in_specs=(
            P("sec", "seq", None),
            P(),
            P(None, None, "trk"),
            P(None, "trk", None, None),
            P("sec", "seq", "trk", None, None),
            P("trk", None),
            P("sec"),
        ),
        out_specs=(P(("sec", "seq"), None, "trk"), P(("sec", "seq"), "trk", None, None)),
        check_vma=False,
    )
```

```python
import math

import jax
import jax.numpy as jnp
from jax import lax
from jax.sharding import PartitionSpec as P

HTRACKS = 7611
MTRACKS = 2608
DILATION_BINS = 16
HTILES = 60


grad_clip = 0.1


def padded(cells, sides, width):
    for axis, dim in sides:
        count = lax.axis_size(axis)
        ends = count - 1
        head = lax.slice_in_dim(cells, 0, width, axis=dim)
        tail = lax.slice_in_dim(cells, cells.shape[dim] - width, cells.shape[dim], axis=dim)
        cells = jnp.concatenate(
            [
                lax.ppermute(tail, axis, [(i, (i + 1) % count) for i in range(ends)]),
                cells,
                lax.ppermute(head, axis, [((i + 1) % count, i) for i in range(ends)]),
            ],
            axis=dim,
        )
    return cells


def contracted_rows(left, right):
    return lax.dot_general(
        left, right, (((0,), (0,)), ((), ())), preferred_element_type=jnp.float32
    )


def body(tokens, norm_gain, dilated_conv_weight, head_weight, targets, owner_tiles, species):
    sample_count = tokens.shape[0]
    local_rows = tokens.shape[1]
    width_all = tokens.shape[2]
    tap_count = dilated_conv_weight.shape[1]
    out_share = dilated_conv_weight.shape[2]
    slot_count = head_weight.shape[2]
    lane_count = head_weight.shape[3]
    inputs = tokens.astype(jnp.float32)
    mean_sq = jnp.mean(inputs * inputs, axis=-1, keepdims=True)
    normed = inputs * lax.rsqrt(mean_sq + 1e-06) * norm_gain.astype(jnp.float32)
    hidden_state = jax.nn.gelu(normed).astype(jnp.bfloat16)
    padded_input = padded(hidden_state, (("seq", 1),), DILATION_BINS)
    convolution_output = jnp.zeros((sample_count, local_rows, out_share), jnp.float32)
    for kernel_tap_index in range(tap_count):
        convolution_output = convolution_output + jnp.dot(
            padded_input[
                :, kernel_tap_index * DILATION_BINS : kernel_tap_index * DILATION_BINS + local_rows
            ],
            dilated_conv_weight[:, kernel_tap_index, :],
            preferred_element_type=jnp.float32,
        )
    own_cols = lax.dynamic_slice_in_dim(inputs, lax.axis_index("trk") * out_share, out_share, 2)
    mixed_share = (own_cols + convolution_output).astype(jnp.bfloat16)
    mixed_parts = lax.all_gather(mixed_share, "trk", axis=0, tiled=False)
    mixed_all = jnp.transpose(mixed_parts, (1, 2, 0, 3)).reshape(sample_count, local_rows, width_all)
    tiles_here = owner_tiles[0]
    is_mouse = tiles_here >= HTILES
    within = jnp.where(is_mouse, tiles_here - HTILES, tiles_here)
    track_limit = jnp.where(is_mouse, MTRACKS, HTRACKS).astype(jnp.int32)
    lane_ids = jnp.arange(lane_count, dtype=jnp.int32)
    lane_mask = (within[:, None] * lane_count + lane_ids[None, :] < track_limit[:, None]).astype(
        jnp.float32
    )
    grad_scale = 1.0 / math.sqrt(
        lax.axis_size("sec") * sample_count * lax.axis_size("seq") * local_rows
    )
    weights_here = head_weight[:, 0].reshape(width_all, slot_count * lane_count)
    flat_mixed = mixed_all.reshape(sample_count * local_rows, width_all)
    logits = jnp.dot(flat_mixed, weights_here, preferred_element_type=jnp.float32)
    target_cols = targets[:, :, 0].reshape(sample_count * local_rows, slot_count * lane_count)
    active = (tiles_here[None, :] >= 0) & (is_mouse[None, :] == (species[:, None] == 1))
    live_mask = active.astype(jnp.float32)[:, :, None] * lane_mask[None, :, :]
    live_rows = jnp.broadcast_to(
        live_mask.reshape(sample_count, 1, slot_count * lane_count),
        (sample_count, local_rows, slot_count * lane_count),
    ).reshape(sample_count * local_rows, slot_count * lane_count)
    delta_f = (
        grad_scale
        * (jax.nn.softplus(logits) - target_cols.astype(jnp.float32))
        * jax.nn.sigmoid(logits)
        * live_rows
    )
    flat_deltas = delta_f.astype(jnp.bfloat16)
    back_sum = lax.dot_general(
        flat_deltas, weights_here, (((1,), (1,)), ((), ())), preferred_element_type=jnp.float32
    ).reshape(sample_count, local_rows, width_all)
    backward_portion = lax.psum_scatter(back_sum, "trk", scatter_dimension=2, tiled=True).astype(
        jnp.bfloat16
    )
    group_count = lax.axis_size("sec") * lax.axis_size("seq")
    share_rows = width_all // group_count
    hidden_parts = lax.all_to_all(
        padded_input.reshape(sample_count, local_rows + 2 * DILATION_BINS, group_count, share_rows),
        ("sec", "seq"),
        2,
        0,
        tiled=False,
    )
    back_parts = lax.all_gather(backward_portion, ("sec", "seq"), axis=0, tiled=False)
    per_tap = [
        lax.dot_general(
            hidden_parts[
                :, :, kernel_tap_index * DILATION_BINS : kernel_tap_index * DILATION_BINS + local_rows
            ].reshape(group_count, sample_count, local_rows, share_rows),
            back_parts,
            (((0, 1, 2), (0, 1, 2)), ((), ())),
            preferred_element_type=jnp.float32,
        )
        for kernel_tap_index in range(tap_count)
    ]
    conv_grad = jnp.stack(per_tap, axis=1)
    grad_share = lax.psum_scatter(
        contracted_rows(flat_mixed, flat_deltas), ("sec", "seq"), scatter_dimension=0, tiled=True
    )
    total_sq = lax.psum(lax.psum(lax.psum(jnp.sum(grad_share * grad_share), "trk"), "seq"), "sec")
    entries = width_all * lax.axis_size("trk") * slot_count * lane_count
    factor = jnp.minimum(1.0, grad_clip * lax.rsqrt(total_sq / entries + 1e-06))
    head_grad = (grad_share * factor).reshape(share_rows, 1, slot_count, lane_count)
    return (conv_grad, head_grad)


def solution(mesh):
    return jax.shard_map(
        body,
        mesh=mesh,
        in_specs=(
            P("sec", "seq", None),
            P(),
            P(None, None, "trk"),
            P(None, "trk", None, None),
            P("sec", "seq", "trk", None, None),
            P("trk", None),
            P("sec"),
        ),
        out_specs=(P(("sec", "seq"), None, "trk"), P(("sec", "seq"), "trk", None, None)),
        check_vma=False,
    )
```

```python
import math

import jax
import jax.numpy as jnp
from jax import lax
from jax.sharding import PartitionSpec as P

HTRACKS = 7611
MTRACKS = 2608
DILATION_BINS = 16
HTILES = 60


grad_clip = 0.1


def padded(cells, sides, width):
    for axis, dim in sides:
        count = lax.axis_size(axis)
        ends = count - 1
        head = lax.slice_in_dim(cells, 0, width, axis=dim)
        tail = lax.slice_in_dim(cells, cells.shape[dim] - width, cells.shape[dim], axis=dim)
        cells = jnp.concatenate(
            [
                lax.ppermute(tail, axis, [(i, (i + 1) % count) for i in range(ends)]),
                cells,
                lax.ppermute(head, axis, [((i + 1) % count, i) for i in range(ends)]),
            ],
            axis=dim,
        )
    return cells


def contracted_rows(left, right):
    return lax.dot_general(
        left, right, (((0,), (0,)), ((), ())), preferred_element_type=jnp.float32
    )


def body(tokens, norm_gain, dilated_conv_weight, head_weight, targets, owner_tiles, species):
    sample_count = tokens.shape[0]
    local_rows = tokens.shape[1]
    width_all = tokens.shape[2]
    tap_count = dilated_conv_weight.shape[1]
    out_share = dilated_conv_weight.shape[2]
    slot_count = head_weight.shape[2]
    lane_count = head_weight.shape[3]
    inputs = tokens.astype(jnp.float32)
    mean_sq = jnp.mean(inputs * inputs, axis=-1, keepdims=True)
    normed = inputs * lax.rsqrt(mean_sq + 1e-06) * norm_gain.astype(jnp.float32)
    hidden_state = jax.nn.gelu(normed).astype(jnp.bfloat16)
    padded_input = padded(hidden_state, (("seq", 1),), DILATION_BINS)
    convolution_output = jnp.zeros((sample_count, local_rows, out_share), jnp.float32)
    for kernel_tap_index in range(tap_count):
        convolution_output = convolution_output + jnp.dot(
            padded_input[
                :, kernel_tap_index * DILATION_BINS : kernel_tap_index * DILATION_BINS + local_rows
            ],
            dilated_conv_weight[:, kernel_tap_index, :],
            preferred_element_type=jnp.float32,
        )
    own_cols = lax.dynamic_slice_in_dim(inputs, lax.axis_index("trk") * out_share, out_share, 2)
    mixed_share = (own_cols + convolution_output).astype(jnp.bfloat16)
    mixed_parts = lax.all_gather(mixed_share, "trk", axis=0, tiled=False)
    mixed_all = jnp.transpose(mixed_parts, (1, 2, 0, 3)).reshape(sample_count, local_rows, width_all)
    tiles_here = owner_tiles[0]
    is_mouse = tiles_here >= HTILES
    within = jnp.where(is_mouse, tiles_here - HTILES, tiles_here)
    track_limit = jnp.where(is_mouse, MTRACKS, HTRACKS).astype(jnp.int32)
    lane_ids = jnp.arange(lane_count, dtype=jnp.int32)
    lane_mask = (within[:, None] * lane_count + lane_ids[None, :] < track_limit[:, None]).astype(
        jnp.float32
    )
    grad_scale = 1.0 / math.sqrt(
        lax.axis_size("sec") * sample_count * lax.axis_size("seq") * local_rows
    )
    weights_here = head_weight[:, 0].reshape(width_all, slot_count * lane_count)
    flat_mixed = mixed_all.reshape(sample_count * local_rows, width_all)
    logits = jnp.dot(flat_mixed, weights_here, preferred_element_type=jnp.float32)
    target_cols = targets[:, :, 0].reshape(sample_count * local_rows, slot_count * lane_count)
    active = (tiles_here[None, :] >= 0) & (is_mouse[None, :] == (species[:, None] == 1))
    live_mask = active.astype(jnp.float32)[:, :, None] * lane_mask[None, :, :]
    live_rows = jnp.broadcast_to(
        live_mask.reshape(sample_count, 1, slot_count * lane_count),
        (sample_count, local_rows, slot_count * lane_count),
    ).reshape(sample_count * local_rows, slot_count * lane_count)
    delta_f = (
        grad_scale
        * (jax.nn.softplus(logits) - target_cols.astype(jnp.float32))
        * jax.nn.sigmoid(logits)
        * live_rows
    )
    flat_deltas = delta_f.astype(jnp.bfloat16)
    head_partial = contracted_rows(flat_mixed, flat_deltas)
    deltas_for_back, head_partial = lax.optimization_barrier((flat_deltas, head_partial))
    grad_share = lax.psum_scatter(head_partial, ("sec", "seq"), scatter_dimension=0, tiled=True)
    back_sum = lax.dot_general(
        deltas_for_back, weights_here, (((1,), (1,)), ((), ())), preferred_element_type=jnp.float32
    ).reshape(sample_count, local_rows, lax.axis_size("trk"), out_share)
    back_from_owners = lax.all_to_all(back_sum, "trk", 2, 0, tiled=False)
    backward_portion = jnp.sum(back_from_owners, axis=0).astype(jnp.bfloat16)
    group_count = lax.axis_size("sec") * lax.axis_size("seq")
    share_rows = width_all // group_count
    hidden_parts = lax.all_to_all(
        padded_input.reshape(sample_count, local_rows + 2 * DILATION_BINS, group_count, share_rows),
        ("sec", "seq"),
        2,
        0,
        tiled=False,
    )
    back_parts = lax.all_to_all(
        jnp.broadcast_to(
            backward_portion[:, :, None, :], (sample_count, local_rows, group_count, out_share)
        ),
        ("sec", "seq"),
        2,
        0,
        tiled=False,
    )
    per_tap = [
        lax.dot_general(
            hidden_parts[
                :, :, kernel_tap_index * DILATION_BINS : kernel_tap_index * DILATION_BINS + local_rows
            ].reshape(group_count, sample_count, local_rows, share_rows),
            back_parts,
            (((0, 1, 2), (0, 1, 2)), ((), ())),
            preferred_element_type=jnp.float32,
        )
        for kernel_tap_index in range(tap_count)
    ]
    conv_grad = jnp.stack(per_tap, axis=1)
    total_sq = lax.psum(lax.psum(lax.psum(jnp.sum(grad_share * grad_share), "trk"), "seq"), "sec")
    entries = width_all * lax.axis_size("trk") * slot_count * lane_count
    factor = jnp.minimum(1.0, grad_clip * lax.rsqrt(total_sq / entries + 1e-06))
    head_grad = (grad_share * factor).reshape(share_rows, 1, slot_count, lane_count)
    return (conv_grad, head_grad)


def solution(mesh):
    return jax.shard_map(
        body,
        mesh=mesh,
        in_specs=(
            P("sec", "seq", None),
            P(),
            P(None, None, "trk"),
            P(None, "trk", None, None),
            P("sec", "seq", "trk", None, None),
            P("trk", None),
            P("sec"),
        ),
        out_specs=(P(("sec", "seq"), None, "trk"), P(("sec", "seq"), "trk", None, None)),
        check_vma=False,
    )
```

```python
import math

import jax
import jax.numpy as jnp
from jax import lax
from jax.sharding import PartitionSpec as P

HTRACKS = 7611
MTRACKS = 2608
DILATION_BINS = 16
HTILES = 60


grad_clip = 0.1


def padded(cells, sides, width):
    for axis, dim in sides:
        count = lax.axis_size(axis)
        ends = count - 1
        head = lax.slice_in_dim(cells, 0, width, axis=dim)
        tail = lax.slice_in_dim(cells, cells.shape[dim] - width, cells.shape[dim], axis=dim)
        cells = jnp.concatenate(
            [
                lax.ppermute(tail, axis, [(i, (i + 1) % count) for i in range(ends)]),
                cells,
                lax.ppermute(head, axis, [((i + 1) % count, i) for i in range(ends)]),
            ],
            axis=dim,
        )
    return cells


def contracted_rows(left, right):
    return lax.dot_general(
        left, right, (((0,), (0,)), ((), ())), preferred_element_type=jnp.float32
    )


def ring_scatter(partial):
    rows_all, cols = partial.shape
    sec_n = lax.axis_size("sec")
    x_n = lax.axis_size("seq") // 2
    share = rows_all // (sec_n * x_n * 2)
    sec_i = lax.axis_index("sec")
    x_i = lax.axis_index("seq") // 2
    core_i = lax.axis_index("seq") % 2
    blocks = partial.reshape(sec_n, x_n, 2, share, cols)
    keep = lax.dynamic_index_in_dim(blocks, core_i, 2, keepdims=False)
    give = lax.dynamic_index_in_dim(blocks, 1 - core_i, 2, keepdims=False)
    core_pairs = [(2 * i + j, 2 * i + 1 - j) for i in range(x_n) for j in range(2)]
    summed = keep + lax.ppermute(give, "seq", core_pairs)
    half = cols // 2
    ahead = summed[..., :half]
    behind = summed[..., half:]
    to_next = [(2 * i + j, 2 * ((i + 1) % x_n) + j) for i in range(x_n) for j in range(2)]
    to_prev = [(2 * i + j, 2 * ((i - 1) % x_n) + j) for i in range(x_n) for j in range(2)]
    send_a = lax.dynamic_index_in_dim(ahead, (x_i - 1) % x_n, 1, keepdims=False)
    send_b = lax.dynamic_index_in_dim(behind, (x_i + 1) % x_n, 1, keepdims=False)
    for step in range(x_n - 1):
        got_a = lax.ppermute(send_a, "seq", to_next)
        got_b = lax.ppermute(send_b, "seq", to_prev)
        send_a = got_a + lax.dynamic_index_in_dim(ahead, (x_i - step - 2) % x_n, 1, keepdims=False)
        send_b = got_b + lax.dynamic_index_in_dim(behind, (x_i + step + 2) % x_n, 1, keepdims=False)
    reduced = jnp.concatenate([send_a, send_b], axis=-1)
    total = lax.dynamic_index_in_dim(reduced, sec_i, 0, keepdims=False)
    for shift in range(1, sec_n):
        other = lax.dynamic_index_in_dim(reduced, (sec_i - shift) % sec_n, 0, keepdims=False)
        total = total + lax.ppermute(
            other, "sec", [(i, (i - shift) % sec_n) for i in range(sec_n)]
        )
    return total


def body(tokens, norm_gain, dilated_conv_weight, head_weight, targets, owner_tiles, species):
    sample_count = tokens.shape[0]
    local_rows = tokens.shape[1]
    width_all = tokens.shape[2]
    tap_count = dilated_conv_weight.shape[1]
    out_share = dilated_conv_weight.shape[2]
    slot_count = head_weight.shape[2]
    lane_count = head_weight.shape[3]
    inputs = tokens.astype(jnp.float32)
    mean_sq = jnp.mean(inputs * inputs, axis=-1, keepdims=True)
    normed = inputs * lax.rsqrt(mean_sq + 1e-06) * norm_gain.astype(jnp.float32)
    hidden_state = jax.nn.gelu(normed).astype(jnp.bfloat16)
    padded_input = padded(hidden_state, (("seq", 1),), DILATION_BINS)
    convolution_output = jnp.zeros((sample_count, local_rows, out_share), jnp.float32)
    for kernel_tap_index in range(tap_count):
        convolution_output = convolution_output + jnp.dot(
            padded_input[
                :, kernel_tap_index * DILATION_BINS : kernel_tap_index * DILATION_BINS + local_rows
            ],
            dilated_conv_weight[:, kernel_tap_index, :],
            preferred_element_type=jnp.float32,
        )
    own_cols = lax.dynamic_slice_in_dim(inputs, lax.axis_index("trk") * out_share, out_share, 2)
    mixed_share = (own_cols + convolution_output).astype(jnp.bfloat16)
    mixed_parts = lax.all_gather(mixed_share, "trk", axis=0, tiled=False)
    mixed_all = jnp.transpose(mixed_parts, (1, 2, 0, 3)).reshape(sample_count, local_rows, width_all)
    tiles_here = owner_tiles[0]
    is_mouse = tiles_here >= HTILES
    within = jnp.where(is_mouse, tiles_here - HTILES, tiles_here)
    track_limit = jnp.where(is_mouse, MTRACKS, HTRACKS).astype(jnp.int32)
    lane_ids = jnp.arange(lane_count, dtype=jnp.int32)
    lane_mask = (within[:, None] * lane_count + lane_ids[None, :] < track_limit[:, None]).astype(
        jnp.float32
    )
    grad_scale = 1.0 / math.sqrt(
        lax.axis_size("sec") * sample_count * lax.axis_size("seq") * local_rows
    )
    weights_here = head_weight[:, 0].reshape(width_all, slot_count * lane_count)
    flat_mixed = mixed_all.reshape(sample_count * local_rows, width_all)
    logits = jnp.dot(flat_mixed, weights_here, preferred_element_type=jnp.float32)
    target_cols = targets[:, :, 0].reshape(sample_count * local_rows, slot_count * lane_count)
    active = (tiles_here[None, :] >= 0) & (is_mouse[None, :] == (species[:, None] == 1))
    live_mask = active.astype(jnp.float32)[:, :, None] * lane_mask[None, :, :]
    live_rows = jnp.broadcast_to(
        live_mask.reshape(sample_count, 1, slot_count * lane_count),
        (sample_count, local_rows, slot_count * lane_count),
    ).reshape(sample_count * local_rows, slot_count * lane_count)
    delta_f = (
        grad_scale
        * (jax.nn.softplus(logits) - target_cols.astype(jnp.float32))
        * jax.nn.sigmoid(logits)
        * live_rows
    )
    flat_deltas = delta_f.astype(jnp.bfloat16)
    head_partial = contracted_rows(flat_mixed, flat_deltas)
    deltas_for_back, head_partial = lax.optimization_barrier((flat_deltas, head_partial))
    grad_share = ring_scatter(head_partial)
    back_t = jnp.dot(weights_here, deltas_for_back.T, preferred_element_type=jnp.float32)
    backward_portion = lax.psum_scatter(back_t, "trk", scatter_dimension=0, tiled=True).astype(
        jnp.bfloat16
    )
    group_count = lax.axis_size("sec") * lax.axis_size("seq")
    share_rows = width_all // group_count
    hidden_parts = lax.all_to_all(
        padded_input.reshape(sample_count, local_rows + 2 * DILATION_BINS, group_count, share_rows),
        ("sec", "seq"),
        2,
        0,
        tiled=False,
    )
    back_parts = lax.all_gather(backward_portion, ("sec", "seq"), axis=0, tiled=False)
    per_tap = [
        lax.dot_general(
            hidden_parts[
                :, :, kernel_tap_index * DILATION_BINS : kernel_tap_index * DILATION_BINS + local_rows
            ].reshape(group_count, sample_count * local_rows, share_rows),
            back_parts,
            (((0, 1), (0, 2)), ((), ())),
            preferred_element_type=jnp.float32,
        )
        for kernel_tap_index in range(tap_count)
    ]
    conv_grad = jnp.stack(per_tap, axis=1)
    total_sq = lax.psum(lax.psum(lax.psum(jnp.sum(grad_share * grad_share), "trk"), "seq"), "sec")
    entries = width_all * lax.axis_size("trk") * slot_count * lane_count
    factor = jnp.minimum(1.0, grad_clip * lax.rsqrt(total_sq / entries + 1e-06))
    head_grad = (grad_share * factor).reshape(share_rows, 1, slot_count, lane_count)
    return (conv_grad, head_grad)


def solution(mesh):
    return jax.shard_map(
        body,
        mesh=mesh,
        in_specs=(
            P("sec", "seq", None),
            P(),
            P(None, None, "trk"),
            P(None, "trk", None, None),
            P("sec", "seq", "trk", None, None),
            P("trk", None),
            P("sec"),
        ),
        out_specs=(P(("sec", "seq"), None, "trk"), P(("sec", "seq"), "trk", None, None)),
        check_vma=False,
    )
```

```python
import math

import jax
import jax.numpy as jnp
from jax import lax
from jax.sharding import PartitionSpec as P

HTRACKS = 7611
MTRACKS = 2608
DILATION_BINS = 16
HTILES = 60


grad_clip = 0.1


def padded(cells, sides, width):
    for axis, dim in sides:
        count = lax.axis_size(axis)
        ends = count - 1
        head = lax.slice_in_dim(cells, 0, width, axis=dim)
        tail = lax.slice_in_dim(cells, cells.shape[dim] - width, cells.shape[dim], axis=dim)
        cells = jnp.concatenate(
            [
                lax.ppermute(tail, axis, [(i, (i + 1) % count) for i in range(ends)]),
                cells,
                lax.ppermute(head, axis, [((i + 1) % count, i) for i in range(ends)]),
            ],
            axis=dim,
        )
    return cells


def contracted_rows(left, right):
    return lax.dot_general(
        left, right, (((0,), (0,)), ((), ())), preferred_element_type=jnp.float32
    )


def ring_scatter(partial):
    rows_all, cols = partial.shape
    sec_n = lax.axis_size("sec")
    x_n = lax.axis_size("seq") // 2
    share = rows_all // (sec_n * x_n * 2)
    sec_i = lax.axis_index("sec")
    x_i = lax.axis_index("seq") // 2
    core_i = lax.axis_index("seq") % 2
    blocks = partial.reshape(sec_n, x_n, 2, share, cols)
    keep = lax.dynamic_index_in_dim(blocks, core_i, 2, keepdims=False)
    give = lax.dynamic_index_in_dim(blocks, 1 - core_i, 2, keepdims=False)
    core_pairs = [(2 * i + j, 2 * i + 1 - j) for i in range(x_n) for j in range(2)]
    summed = keep + lax.ppermute(give, "seq", core_pairs)
    half = cols // 2
    ahead = summed[..., :half]
    behind = summed[..., half:]
    to_next = [(2 * i + j, 2 * ((i + 1) % x_n) + j) for i in range(x_n) for j in range(2)]
    to_prev = [(2 * i + j, 2 * ((i - 1) % x_n) + j) for i in range(x_n) for j in range(2)]
    send_a = lax.dynamic_index_in_dim(ahead, (x_i - 1) % x_n, 1, keepdims=False)
    send_b = lax.dynamic_index_in_dim(behind, (x_i + 1) % x_n, 1, keepdims=False)
    for step in range(x_n - 1):
        got_a = lax.ppermute(send_a, "seq", to_next)
        got_b = lax.ppermute(send_b, "seq", to_prev)
        send_a = got_a + lax.dynamic_index_in_dim(ahead, (x_i - step - 2) % x_n, 1, keepdims=False)
        send_b = got_b + lax.dynamic_index_in_dim(behind, (x_i + step + 2) % x_n, 1, keepdims=False)
    reduced = jnp.concatenate([send_a, send_b], axis=-1)
    total = lax.dynamic_index_in_dim(reduced, sec_i, 0, keepdims=False)
    for shift in range(1, sec_n):
        other = lax.dynamic_index_in_dim(reduced, (sec_i - shift) % sec_n, 0, keepdims=False)
        total = total + lax.ppermute(
            other, "sec", [(i, (i - shift) % sec_n) for i in range(sec_n)]
        )
    return total


def butterfly_sum(value):
    for axis in ("seq", "trk", "sec"):
        count = lax.axis_size(axis)
        bit = 1
        while bit < count:
            value = value + lax.ppermute(value, axis, [(i, i ^ bit) for i in range(count)])
            bit *= 2
    return value


def body(tokens, norm_gain, dilated_conv_weight, head_weight, targets, owner_tiles, species):
    sample_count = tokens.shape[0]
    local_rows = tokens.shape[1]
    width_all = tokens.shape[2]
    tap_count = dilated_conv_weight.shape[1]
    out_share = dilated_conv_weight.shape[2]
    slot_count = head_weight.shape[2]
    lane_count = head_weight.shape[3]
    inputs = tokens.astype(jnp.float32)
    mean_sq = jnp.mean(inputs * inputs, axis=-1, keepdims=True)
    normed = inputs * lax.rsqrt(mean_sq + 1e-06) * norm_gain.astype(jnp.float32)
    hidden_state = jax.nn.gelu(normed).astype(jnp.bfloat16)
    padded_input = padded(hidden_state, (("seq", 1),), DILATION_BINS)
    convolution_output = jnp.zeros((sample_count, local_rows, out_share), jnp.float32)
    for kernel_tap_index in range(tap_count):
        convolution_output = convolution_output + jnp.dot(
            padded_input[
                :, kernel_tap_index * DILATION_BINS : kernel_tap_index * DILATION_BINS + local_rows
            ],
            dilated_conv_weight[:, kernel_tap_index, :],
            preferred_element_type=jnp.float32,
        )
    own_cols = lax.dynamic_slice_in_dim(inputs, lax.axis_index("trk") * out_share, out_share, 2)
    mixed_share = (own_cols + convolution_output).astype(jnp.bfloat16)
    trk_n = lax.axis_size("trk")
    shifted = [mixed_share] + [
        lax.ppermute(mixed_share, "trk", [(i, (i + k) % trk_n) for i in range(trk_n)])
        for k in range(1, trk_n)
    ]
    order = (lax.axis_index("trk") - jnp.arange(trk_n)) % trk_n
    mixed_parts = jnp.take(jnp.stack(shifted), order, axis=0)
    mixed_all = jnp.transpose(mixed_parts, (1, 2, 0, 3)).reshape(sample_count, local_rows, width_all)
    tiles_here = owner_tiles[0]
    is_mouse = tiles_here >= HTILES
    within = jnp.where(is_mouse, tiles_here - HTILES, tiles_here)
    track_limit = jnp.where(is_mouse, MTRACKS, HTRACKS).astype(jnp.int32)
    lane_ids = jnp.arange(lane_count, dtype=jnp.int32)
    lane_mask = (within[:, None] * lane_count + lane_ids[None, :] < track_limit[:, None]).astype(
        jnp.float32
    )
    grad_scale = 1.0 / math.sqrt(
        lax.axis_size("sec") * sample_count * lax.axis_size("seq") * local_rows
    )
    weights_here = head_weight[:, 0].reshape(width_all, slot_count * lane_count)
    flat_mixed = mixed_all.reshape(sample_count * local_rows, width_all)
    logits = jnp.dot(flat_mixed, weights_here, preferred_element_type=jnp.float32)
    target_cols = targets[:, :, 0].reshape(sample_count * local_rows, slot_count * lane_count)
    active = (tiles_here[None, :] >= 0) & (is_mouse[None, :] == (species[:, None] == 1))
    live_mask = active.astype(jnp.float32)[:, :, None] * lane_mask[None, :, :]
    live_rows = jnp.broadcast_to(
        live_mask.reshape(sample_count, 1, slot_count * lane_count),
        (sample_count, local_rows, slot_count * lane_count),
    ).reshape(sample_count * local_rows, slot_count * lane_count)
    delta_f = (
        grad_scale
        * (jax.nn.softplus(logits) - target_cols.astype(jnp.float32))
        * jax.nn.sigmoid(logits)
        * live_rows
    )
    flat_deltas = delta_f.astype(jnp.bfloat16)
    head_partial = contracted_rows(flat_mixed, flat_deltas)
    deltas_for_back, head_partial = lax.optimization_barrier((flat_deltas, head_partial))
    grad_share = ring_scatter(head_partial)
    back_t = jnp.dot(weights_here, deltas_for_back.T, preferred_element_type=jnp.float32)
    backward_portion = lax.psum_scatter(back_t, "trk", scatter_dimension=0, tiled=True).astype(
        jnp.bfloat16
    )
    group_count = lax.axis_size("sec") * lax.axis_size("seq")
    share_rows = width_all // group_count
    hidden_parts = lax.all_to_all(
        padded_input.reshape(sample_count, local_rows + 2 * DILATION_BINS, group_count, share_rows),
        ("sec", "seq"),
        2,
        0,
        tiled=False,
    )
    back_parts = lax.all_gather(backward_portion, ("sec", "seq"), axis=0, tiled=False)
    per_tap = [
        lax.dot_general(
            hidden_parts[
                :, :, kernel_tap_index * DILATION_BINS : kernel_tap_index * DILATION_BINS + local_rows
            ].reshape(group_count, sample_count * local_rows, share_rows),
            back_parts,
            (((0, 1), (0, 2)), ((), ())),
            preferred_element_type=jnp.float32,
        )
        for kernel_tap_index in range(tap_count)
    ]
    conv_grad = jnp.stack(per_tap, axis=1)
    total_sq = butterfly_sum(jnp.sum(grad_share * grad_share))
    entries = width_all * lax.axis_size("trk") * slot_count * lane_count
    factor = jnp.minimum(1.0, grad_clip * lax.rsqrt(total_sq / entries + 1e-06))
    head_grad = (grad_share * factor).reshape(share_rows, 1, slot_count, lane_count)
    return (conv_grad, head_grad)


def solution(mesh):
    return jax.shard_map(
        body,
        mesh=mesh,
        in_specs=(
            P("sec", "seq", None),
            P(),
            P(None, None, "trk"),
            P(None, "trk", None, None),
            P("sec", "seq", "trk", None, None),
            P("trk", None),
            P("sec"),
        ),
        out_specs=(P(("sec", "seq"), None, "trk"), P(("sec", "seq"), "trk", None, None)),
        check_vma=False,
    )
```

```python
import math

import jax
import jax.numpy as jnp
from jax import lax
from jax.sharding import PartitionSpec as P

HTRACKS = 7611
MTRACKS = 2608
DILATION_BINS = 16
HTILES = 60


grad_clip = 0.1


def padded(cells, sides, width):
    for axis, dim in sides:
        count = lax.axis_size(axis)
        ends = count - 1
        head = lax.slice_in_dim(cells, 0, width, axis=dim)
        tail = lax.slice_in_dim(cells, cells.shape[dim] - width, cells.shape[dim], axis=dim)
        cells = jnp.concatenate(
            [
                lax.ppermute(tail, axis, [(i, (i + 1) % count) for i in range(ends)]),
                cells,
                lax.ppermute(head, axis, [((i + 1) % count, i) for i in range(ends)]),
            ],
            axis=dim,
        )
    return cells


def contracted_rows(left, right):
    return lax.dot_general(
        left, right, (((0,), (0,)), ((), ())), preferred_element_type=jnp.float32
    )


def ring_scatter(partial):
    rows_all, cols = partial.shape
    sec_n = lax.axis_size("sec")
    x_n = lax.axis_size("seq") // 2
    share = rows_all // (sec_n * x_n * 2)
    sec_i = lax.axis_index("sec")
    x_i = lax.axis_index("seq") // 2
    core_i = lax.axis_index("seq") % 2
    blocks = partial.reshape(sec_n, x_n, 2, share, cols)
    keep = lax.dynamic_index_in_dim(blocks, core_i, 2, keepdims=False)
    give = lax.dynamic_index_in_dim(blocks, 1 - core_i, 2, keepdims=False)
    core_pairs = [(2 * i + j, 2 * i + 1 - j) for i in range(x_n) for j in range(2)]
    summed = keep + lax.ppermute(give, "seq", core_pairs)
    half = cols // 2
    ahead = summed[..., :half]
    behind = summed[..., half:]
    to_next = [(2 * i + j, 2 * ((i + 1) % x_n) + j) for i in range(x_n) for j in range(2)]
    to_prev = [(2 * i + j, 2 * ((i - 1) % x_n) + j) for i in range(x_n) for j in range(2)]
    send_a = lax.dynamic_index_in_dim(ahead, (x_i - 1) % x_n, 1, keepdims=False)
    send_b = lax.dynamic_index_in_dim(behind, (x_i + 1) % x_n, 1, keepdims=False)
    for step in range(x_n - 1):
        got_a = lax.ppermute(send_a, "seq", to_next)
        got_b = lax.ppermute(send_b, "seq", to_prev)
        send_a = got_a + lax.dynamic_index_in_dim(ahead, (x_i - step - 2) % x_n, 1, keepdims=False)
        send_b = got_b + lax.dynamic_index_in_dim(behind, (x_i + step + 2) % x_n, 1, keepdims=False)
    reduced = jnp.concatenate([send_a, send_b], axis=-1)
    total = lax.dynamic_index_in_dim(reduced, sec_i, 0, keepdims=False)
    for shift in range(1, sec_n):
        other = lax.dynamic_index_in_dim(reduced, (sec_i - shift) % sec_n, 0, keepdims=False)
        total = total + lax.ppermute(
            other, "sec", [(i, (i - shift) % sec_n) for i in range(sec_n)]
        )
    return total


def butterfly_sum(value):
    for axis in ("seq", "trk", "sec"):
        count = lax.axis_size(axis)
        bit = 1
        while bit < count:
            value = value + lax.ppermute(value, axis, [(i, i ^ bit) for i in range(count)])
            bit *= 2
    return value


def body(tokens, norm_gain, dilated_conv_weight, head_weight, targets, owner_tiles, species):
    sample_count = tokens.shape[0]
    local_rows = tokens.shape[1]
    width_all = tokens.shape[2]
    tap_count = dilated_conv_weight.shape[1]
    out_share = dilated_conv_weight.shape[2]
    slot_count = head_weight.shape[2]
    lane_count = head_weight.shape[3]
    inputs = tokens.astype(jnp.float32)
    mean_sq = jnp.mean(inputs * inputs, axis=-1, keepdims=True)
    normed = inputs * lax.rsqrt(mean_sq + 1e-06) * norm_gain.astype(jnp.float32)
    hidden_state = jax.nn.gelu(normed).astype(jnp.bfloat16)
    padded_input = padded(hidden_state, (("seq", 1),), DILATION_BINS)
    convolution_output = jnp.zeros((sample_count, local_rows, out_share), jnp.float32)
    for kernel_tap_index in range(tap_count):
        convolution_output = convolution_output + jnp.dot(
            padded_input[
                :, kernel_tap_index * DILATION_BINS : kernel_tap_index * DILATION_BINS + local_rows
            ],
            dilated_conv_weight[:, kernel_tap_index, :],
            preferred_element_type=jnp.float32,
        )
    own_cols = lax.dynamic_slice_in_dim(inputs, lax.axis_index("trk") * out_share, out_share, 2)
    mixed_share = (own_cols + convolution_output).astype(jnp.bfloat16)
    trk_n = lax.axis_size("trk")
    mixed_parts = lax.all_to_all(
        jnp.broadcast_to(mixed_share[:, :, None, :], (sample_count, local_rows, trk_n, out_share)),
        "trk",
        2,
        0,
        tiled=False,
    )
    mixed_all = jnp.transpose(mixed_parts, (1, 2, 0, 3)).reshape(sample_count, local_rows, width_all)
    tiles_here = owner_tiles[0]
    is_mouse = tiles_here >= HTILES
    within = jnp.where(is_mouse, tiles_here - HTILES, tiles_here)
    track_limit = jnp.where(is_mouse, MTRACKS, HTRACKS).astype(jnp.int32)
    lane_ids = jnp.arange(lane_count, dtype=jnp.int32)
    lane_mask = (within[:, None] * lane_count + lane_ids[None, :] < track_limit[:, None]).astype(
        jnp.float32
    )
    grad_scale = 1.0 / math.sqrt(
        lax.axis_size("sec") * sample_count * lax.axis_size("seq") * local_rows
    )
    weights_here = head_weight[:, 0].reshape(width_all, slot_count * lane_count)
    flat_mixed = mixed_all.reshape(sample_count * local_rows, width_all)
    logits = jnp.dot(flat_mixed, weights_here, preferred_element_type=jnp.float32)
    target_cols = targets[:, :, 0].reshape(sample_count * local_rows, slot_count * lane_count)
    active = (tiles_here[None, :] >= 0) & (is_mouse[None, :] == (species[:, None] == 1))
    live_mask = active.astype(jnp.float32)[:, :, None] * lane_mask[None, :, :]
    live_rows = jnp.broadcast_to(
        live_mask.reshape(sample_count, 1, slot_count * lane_count),
        (sample_count, local_rows, slot_count * lane_count),
    ).reshape(sample_count * local_rows, slot_count * lane_count)
    delta_f = (
        grad_scale
        * (jax.nn.softplus(logits) - target_cols.astype(jnp.float32))
        * jax.nn.sigmoid(logits)
        * live_rows
    )
    flat_deltas = delta_f.astype(jnp.bfloat16)
    head_partial = contracted_rows(flat_mixed, flat_deltas)
    deltas_for_back, head_partial = lax.optimization_barrier((flat_deltas, head_partial))
    grad_share = ring_scatter(head_partial)
    back_t = jnp.dot(weights_here, deltas_for_back.T, preferred_element_type=jnp.float32)
    backward_portion = lax.psum_scatter(back_t, "trk", scatter_dimension=0, tiled=True).astype(
        jnp.bfloat16
    )
    group_count = lax.axis_size("sec") * lax.axis_size("seq")
    share_rows = width_all // group_count
    hidden_parts = lax.all_to_all(
        padded_input.reshape(sample_count, local_rows + 2 * DILATION_BINS, group_count, share_rows),
        ("sec", "seq"),
        2,
        0,
        tiled=False,
    )
    back_parts = lax.all_gather(backward_portion, ("sec", "seq"), axis=0, tiled=False)
    per_tap = [
        lax.dot_general(
            hidden_parts[
                :, :, kernel_tap_index * DILATION_BINS : kernel_tap_index * DILATION_BINS + local_rows
            ].reshape(group_count, sample_count * local_rows, share_rows),
            back_parts,
            (((0, 1), (0, 2)), ((), ())),
            preferred_element_type=jnp.float32,
        )
        for kernel_tap_index in range(tap_count)
    ]
    conv_grad = jnp.stack(per_tap, axis=1)
    all_axes = ("sec", "seq", "trk")
    device_count = lax.axis_size(all_axes)
    sq_parts = lax.all_to_all(
        jnp.broadcast_to(jnp.sum(grad_share * grad_share), (device_count,)), all_axes, 0, 0, tiled=True
    )
    total_sq = jnp.sum(sq_parts)
    entries = width_all * lax.axis_size("trk") * slot_count * lane_count
    factor = jnp.minimum(1.0, grad_clip * lax.rsqrt(total_sq / entries + 1e-06))
    head_grad = (grad_share * factor).reshape(share_rows, 1, slot_count, lane_count)
    return (conv_grad, head_grad)


def solution(mesh):
    return jax.shard_map(
        body,
        mesh=mesh,
        in_specs=(
            P("sec", "seq", None),
            P(),
            P(None, None, "trk"),
            P(None, "trk", None, None),
            P("sec", "seq", "trk", None, None),
            P("trk", None),
            P("sec"),
        ),
        out_specs=(P(("sec", "seq"), None, "trk"), P(("sec", "seq"), "trk", None, None)),
        check_vma=False,
    )
```

```python
import math

import jax
import jax.numpy as jnp
from jax import lax
from jax.sharding import PartitionSpec as P

HTRACKS = 7611
MTRACKS = 2608
DILATION_BINS = 16
HTILES = 60


grad_clip = 0.1


def padded(cells, sides, width):
    for axis, dim in sides:
        count = lax.axis_size(axis)
        ends = count - 1
        head = lax.slice_in_dim(cells, 0, width, axis=dim)
        tail = lax.slice_in_dim(cells, cells.shape[dim] - width, cells.shape[dim], axis=dim)
        cells = jnp.concatenate(
            [
                lax.ppermute(tail, axis, [(i, (i + 1) % count) for i in range(ends)]),
                cells,
                lax.ppermute(head, axis, [((i + 1) % count, i) for i in range(ends)]),
            ],
            axis=dim,
        )
    return cells


def contracted_rows(left, right):
    return lax.dot_general(
        left, right, (((0,), (0,)), ((), ())), preferred_element_type=jnp.float32
    )


def core_halves(rows):
    count, width = rows.shape
    sec_n = lax.axis_size("sec")
    x_n = lax.axis_size("seq") // 2
    core_i = lax.axis_index("seq") % 2
    grouped = rows.reshape(count, sec_n, x_n, 2, width // (sec_n * x_n * 2))
    keep = lax.dynamic_index_in_dim(grouped, core_i, 3, keepdims=False).reshape(count, width // 2)
    give = lax.dynamic_index_in_dim(grouped, 1 - core_i, 3, keepdims=False).reshape(count, width // 2)
    return keep, give


def ring_scatter(keep, give):
    rows_half, cols = keep.shape
    sec_n = lax.axis_size("sec")
    x_n = lax.axis_size("seq") // 2
    share = rows_half // (sec_n * x_n)
    sec_i = lax.axis_index("sec")
    x_i = lax.axis_index("seq") // 2
    keep = keep.reshape(sec_n, x_n, share, cols)
    give = give.reshape(sec_n, x_n, share, cols)
    core_pairs = [(2 * i + j, 2 * i + 1 - j) for i in range(x_n) for j in range(2)]
    summed = keep + lax.ppermute(give, "seq", core_pairs)
    half = cols // 2
    ahead = summed[..., :half]
    behind = summed[..., half:]
    to_next = [(2 * i + j, 2 * ((i + 1) % x_n) + j) for i in range(x_n) for j in range(2)]
    to_prev = [(2 * i + j, 2 * ((i - 1) % x_n) + j) for i in range(x_n) for j in range(2)]
    send_a = lax.dynamic_index_in_dim(ahead, (x_i - 1) % x_n, 1, keepdims=False)
    send_b = lax.dynamic_index_in_dim(behind, (x_i + 1) % x_n, 1, keepdims=False)
    for step in range(x_n - 1):
        got_a = lax.ppermute(send_a, "seq", to_next)
        got_b = lax.ppermute(send_b, "seq", to_prev)
        send_a = got_a + lax.dynamic_index_in_dim(ahead, (x_i - step - 2) % x_n, 1, keepdims=False)
        send_b = got_b + lax.dynamic_index_in_dim(behind, (x_i + step + 2) % x_n, 1, keepdims=False)
    reduced = jnp.concatenate([send_a, send_b], axis=-1)
    total = lax.dynamic_index_in_dim(reduced, sec_i, 0, keepdims=False)
    for shift in range(1, sec_n):
        other = lax.dynamic_index_in_dim(reduced, (sec_i - shift) % sec_n, 0, keepdims=False)
        total = total + lax.ppermute(
            other, "sec", [(i, (i - shift) % sec_n) for i in range(sec_n)]
        )
    return total


def butterfly_sum(value):
    for axis in ("seq", "trk", "sec"):
        count = lax.axis_size(axis)
        bit = 1
        while bit < count:
            value = value + lax.ppermute(value, axis, [(i, i ^ bit) for i in range(count)])
            bit *= 2
    return value


def body(tokens, norm_gain, dilated_conv_weight, head_weight, targets, owner_tiles, species):
    sample_count = tokens.shape[0]
    local_rows = tokens.shape[1]
    width_all = tokens.shape[2]
    tap_count = dilated_conv_weight.shape[1]
    out_share = dilated_conv_weight.shape[2]
    slot_count = head_weight.shape[2]
    lane_count = head_weight.shape[3]
    inputs = tokens.astype(jnp.float32)
    mean_sq = jnp.mean(inputs * inputs, axis=-1, keepdims=True)
    normed = inputs * lax.rsqrt(mean_sq + 1e-06) * norm_gain.astype(jnp.float32)
    hidden_state = jax.nn.gelu(normed).astype(jnp.bfloat16)
    padded_input = padded(hidden_state, (("seq", 1),), DILATION_BINS)
    convolution_output = jnp.zeros((sample_count, local_rows, out_share), jnp.float32)
    for kernel_tap_index in range(tap_count):
        convolution_output = convolution_output + jnp.dot(
            padded_input[
                :, kernel_tap_index * DILATION_BINS : kernel_tap_index * DILATION_BINS + local_rows
            ],
            dilated_conv_weight[:, kernel_tap_index, :],
            preferred_element_type=jnp.float32,
        )
    own_cols = lax.dynamic_slice_in_dim(inputs, lax.axis_index("trk") * out_share, out_share, 2)
    mixed_share = (own_cols + convolution_output).astype(jnp.bfloat16)
    trk_n = lax.axis_size("trk")
    mixed_parts = lax.all_to_all(
        jnp.broadcast_to(mixed_share[:, :, None, :], (sample_count, local_rows, trk_n, out_share)),
        "trk",
        2,
        0,
        tiled=False,
    )
    mixed_all = jnp.transpose(mixed_parts, (1, 2, 0, 3)).reshape(sample_count, local_rows, width_all)
    tiles_here = owner_tiles[0]
    is_mouse = tiles_here >= HTILES
    within = jnp.where(is_mouse, tiles_here - HTILES, tiles_here)
    track_limit = jnp.where(is_mouse, MTRACKS, HTRACKS).astype(jnp.int32)
    lane_ids = jnp.arange(lane_count, dtype=jnp.int32)
    lane_mask = (within[:, None] * lane_count + lane_ids[None, :] < track_limit[:, None]).astype(
        jnp.float32
    )
    grad_scale = 1.0 / math.sqrt(
        lax.axis_size("sec") * sample_count * lax.axis_size("seq") * local_rows
    )
    weights_here = head_weight[:, 0].reshape(width_all, slot_count * lane_count)
    flat_mixed = mixed_all.reshape(sample_count * local_rows, width_all)
    logits = jnp.dot(flat_mixed, weights_here, preferred_element_type=jnp.float32)
    target_cols = targets[:, :, 0].reshape(sample_count * local_rows, slot_count * lane_count)
    active = (tiles_here[None, :] >= 0) & (is_mouse[None, :] == (species[:, None] == 1))
    live_mask = active.astype(jnp.float32)[:, :, None] * lane_mask[None, :, :]
    live_rows = jnp.broadcast_to(
        live_mask.reshape(sample_count, 1, slot_count * lane_count),
        (sample_count, local_rows, slot_count * lane_count),
    ).reshape(sample_count * local_rows, slot_count * lane_count)
    delta_f = (
        grad_scale
        * (jax.nn.softplus(logits) - target_cols.astype(jnp.float32))
        * jax.nn.sigmoid(logits)
        * live_rows
    )
    flat_deltas = delta_f.astype(jnp.bfloat16)
    mixed_keep, mixed_give = core_halves(flat_mixed)
    head_give = contracted_rows(mixed_give, flat_deltas)
    deltas_for_back, head_give = lax.optimization_barrier((flat_deltas, head_give))
    head_keep = contracted_rows(mixed_keep, flat_deltas)
    grad_share = ring_scatter(head_keep, head_give)
    back_t = jnp.dot(weights_here, deltas_for_back.T, preferred_element_type=jnp.float32)
    backward_portion = lax.psum_scatter(back_t, "trk", scatter_dimension=0, tiled=True).astype(
        jnp.bfloat16
    )
    group_count = lax.axis_size("sec") * lax.axis_size("seq")
    share_rows = width_all // group_count
    hidden_parts = lax.all_to_all(
        padded_input.reshape(sample_count, local_rows + 2 * DILATION_BINS, group_count, share_rows),
        ("sec", "seq"),
        2,
        0,
        tiled=False,
    )
    back_parts = lax.all_gather(backward_portion, ("sec", "seq"), axis=0, tiled=False)
    per_tap = [
        lax.dot_general(
            hidden_parts[
                :, :, kernel_tap_index * DILATION_BINS : kernel_tap_index * DILATION_BINS + local_rows
            ].reshape(group_count, sample_count * local_rows, share_rows),
            back_parts,
            (((0, 1), (0, 2)), ((), ())),
            preferred_element_type=jnp.float32,
        )
        for kernel_tap_index in range(tap_count)
    ]
    conv_grad = jnp.stack(per_tap, axis=1)
    all_axes = ("sec", "seq", "trk")
    device_count = lax.axis_size(all_axes)
    sq_parts = lax.all_to_all(
        jnp.broadcast_to(jnp.sum(grad_share * grad_share), (device_count,)), all_axes, 0, 0, tiled=True
    )
    total_sq = jnp.sum(sq_parts)
    entries = width_all * lax.axis_size("trk") * slot_count * lane_count
    factor = jnp.minimum(1.0, grad_clip * lax.rsqrt(total_sq / entries + 1e-06))
    head_grad = (grad_share * factor).reshape(share_rows, 1, slot_count, lane_count)
    return (conv_grad, head_grad)


def solution(mesh):
    return jax.shard_map(
        body,
        mesh=mesh,
        in_specs=(
            P("sec", "seq", None),
            P(),
            P(None, None, "trk"),
            P(None, "trk", None, None),
            P("sec", "seq", "trk", None, None),
            P("trk", None),
            P("sec"),
        ),
        out_specs=(P(("sec", "seq"), None, "trk"), P(("sec", "seq"), "trk", None, None)),
        check_vma=False,
    )
```

```python
import math

import jax
import jax.numpy as jnp
from jax import lax
from jax.sharding import PartitionSpec as P

HTRACKS = 7611
MTRACKS = 2608
DILATION_BINS = 16
HTILES = 60


grad_clip = 0.1


def padded(cells, sides, width):
    for axis, dim in sides:
        count = lax.axis_size(axis)
        ends = count - 1
        head = lax.slice_in_dim(cells, 0, width, axis=dim)
        tail = lax.slice_in_dim(cells, cells.shape[dim] - width, cells.shape[dim], axis=dim)
        cells = jnp.concatenate(
            [
                lax.ppermute(tail, axis, [(i, (i + 1) % count) for i in range(ends)]),
                cells,
                lax.ppermute(head, axis, [((i + 1) % count, i) for i in range(ends)]),
            ],
            axis=dim,
        )
    return cells


def contracted_rows(left, right):
    return lax.dot_general(
        left, right, (((0,), (0,)), ((), ())), preferred_element_type=jnp.float32
    )


def ring_scatter(partial):
    rows_all, cols = partial.shape
    sec_n = lax.axis_size("sec")
    x_n = lax.axis_size("seq") // 2
    share = rows_all // (sec_n * x_n * 2)
    sec_i = lax.axis_index("sec")
    x_i = lax.axis_index("seq") // 2
    core_i = lax.axis_index("seq") % 2
    blocks = partial.reshape(sec_n, x_n, 2, share, cols)
    keep = lax.dynamic_index_in_dim(blocks, core_i, 2, keepdims=False)
    give = lax.dynamic_index_in_dim(blocks, 1 - core_i, 2, keepdims=False)
    core_pairs = [(2 * i + j, 2 * i + 1 - j) for i in range(x_n) for j in range(2)]
    summed = keep + lax.ppermute(give, "seq", core_pairs)
    to_next = [(2 * i + j, 2 * ((i + 1) % x_n) + j) for i in range(x_n) for j in range(2)]
    to_prev = [(2 * i + j, 2 * ((i - 1) % x_n) + j) for i in range(x_n) for j in range(2)]

    def x_ring(data, axis):
        quarter = data.shape[-1] // 2
        ahead = data[..., :quarter]
        behind = data[..., quarter:]
        send_a = lax.dynamic_index_in_dim(ahead, (x_i - 1) % x_n, axis, keepdims=False)
        send_b = lax.dynamic_index_in_dim(behind, (x_i + 1) % x_n, axis, keepdims=False)
        for step in range(x_n - 1):
            got_a = lax.ppermute(send_a, "seq", to_next)
            got_b = lax.ppermute(send_b, "seq", to_prev)
            send_a = got_a + lax.dynamic_index_in_dim(
                ahead, (x_i - step - 2) % x_n, axis, keepdims=False
            )
            send_b = got_b + lax.dynamic_index_in_dim(
                behind, (x_i + step + 2) % x_n, axis, keepdims=False
            )
        return jnp.concatenate([send_a, send_b], axis=-1)

    def sec_pair(data):
        total = lax.dynamic_index_in_dim(data, sec_i, 0, keepdims=False)
        for shift in range(1, sec_n):
            other = lax.dynamic_index_in_dim(data, (sec_i - shift) % sec_n, 0, keepdims=False)
            total = total + lax.ppermute(
                other, "sec", [(i, (i - shift) % sec_n) for i in range(sec_n)]
            )
        return total

    half = cols // 2
    first = sec_pair(x_ring(summed[..., :half], 1))
    second = x_ring(sec_pair(summed[..., half:]), 0)
    return jnp.concatenate([first, second], axis=-1)


def butterfly_sum(value):
    for axis in ("seq", "trk", "sec"):
        count = lax.axis_size(axis)
        bit = 1
        while bit < count:
            value = value + lax.ppermute(value, axis, [(i, i ^ bit) for i in range(count)])
            bit *= 2
    return value


def body(tokens, norm_gain, dilated_conv_weight, head_weight, targets, owner_tiles, species):
    sample_count = tokens.shape[0]
    local_rows = tokens.shape[1]
    width_all = tokens.shape[2]
    tap_count = dilated_conv_weight.shape[1]
    out_share = dilated_conv_weight.shape[2]
    slot_count = head_weight.shape[2]
    lane_count = head_weight.shape[3]
    inputs = tokens.astype(jnp.float32)
    mean_sq = jnp.mean(inputs * inputs, axis=-1, keepdims=True)
    normed = inputs * lax.rsqrt(mean_sq + 1e-06) * norm_gain.astype(jnp.float32)
    hidden_state = jax.nn.gelu(normed).astype(jnp.bfloat16)
    padded_input = padded(hidden_state, (("seq", 1),), DILATION_BINS)
    convolution_output = jnp.zeros((sample_count, local_rows, out_share), jnp.float32)
    for kernel_tap_index in range(tap_count):
        convolution_output = convolution_output + jnp.dot(
            padded_input[
                :, kernel_tap_index * DILATION_BINS : kernel_tap_index * DILATION_BINS + local_rows
            ],
            dilated_conv_weight[:, kernel_tap_index, :],
            preferred_element_type=jnp.float32,
        )
    own_cols = lax.dynamic_slice_in_dim(inputs, lax.axis_index("trk") * out_share, out_share, 2)
    mixed_share = (own_cols + convolution_output).astype(jnp.bfloat16)
    trk_n = lax.axis_size("trk")
    mixed_parts = lax.all_to_all(
        jnp.broadcast_to(mixed_share[:, :, None, :], (sample_count, local_rows, trk_n, out_share)),
        "trk",
        2,
        0,
        tiled=False,
    )
    mixed_all = jnp.transpose(mixed_parts, (1, 2, 0, 3)).reshape(sample_count, local_rows, width_all)
    tiles_here = owner_tiles[0]
    is_mouse = tiles_here >= HTILES
    within = jnp.where(is_mouse, tiles_here - HTILES, tiles_here)
    track_limit = jnp.where(is_mouse, MTRACKS, HTRACKS).astype(jnp.int32)
    lane_ids = jnp.arange(lane_count, dtype=jnp.int32)
    lane_mask = (within[:, None] * lane_count + lane_ids[None, :] < track_limit[:, None]).astype(
        jnp.float32
    )
    grad_scale = 1.0 / math.sqrt(
        lax.axis_size("sec") * sample_count * lax.axis_size("seq") * local_rows
    )
    weights_here = head_weight[:, 0].reshape(width_all, slot_count * lane_count)
    flat_mixed = mixed_all.reshape(sample_count * local_rows, width_all)
    logits = jnp.dot(flat_mixed, weights_here, preferred_element_type=jnp.float32)
    target_cols = targets[:, :, 0].reshape(sample_count * local_rows, slot_count * lane_count)
    active = (tiles_here[None, :] >= 0) & (is_mouse[None, :] == (species[:, None] == 1))
    live_mask = active.astype(jnp.float32)[:, :, None] * lane_mask[None, :, :]
    live_rows = jnp.broadcast_to(
        live_mask.reshape(sample_count, 1, slot_count * lane_count),
        (sample_count, local_rows, slot_count * lane_count),
    ).reshape(sample_count * local_rows, slot_count * lane_count)
    delta_f = (
        grad_scale
        * (jax.nn.softplus(logits) - target_cols.astype(jnp.float32))
        * jax.nn.sigmoid(logits)
        * live_rows
    )
    flat_deltas = delta_f.astype(jnp.bfloat16)
    head_partial = contracted_rows(flat_mixed, flat_deltas)
    deltas_for_back, head_partial = lax.optimization_barrier((flat_deltas, head_partial))
    grad_share = ring_scatter(head_partial)
    back_t = jnp.dot(weights_here, deltas_for_back.T, preferred_element_type=jnp.float32)
    backward_portion = lax.psum_scatter(back_t, "trk", scatter_dimension=0, tiled=True).astype(
        jnp.bfloat16
    )
    group_count = lax.axis_size("sec") * lax.axis_size("seq")
    share_rows = width_all // group_count
    hidden_parts = lax.all_to_all(
        padded_input.reshape(sample_count, local_rows + 2 * DILATION_BINS, group_count, share_rows),
        ("sec", "seq"),
        2,
        0,
        tiled=False,
    )
    back_parts = lax.all_gather(backward_portion, ("sec", "seq"), axis=0, tiled=False)
    per_tap = [
        lax.dot_general(
            hidden_parts[
                :, :, kernel_tap_index * DILATION_BINS : kernel_tap_index * DILATION_BINS + local_rows
            ].reshape(group_count, sample_count * local_rows, share_rows),
            back_parts,
            (((0, 1), (0, 2)), ((), ())),
            preferred_element_type=jnp.float32,
        )
        for kernel_tap_index in range(tap_count)
    ]
    conv_grad = jnp.stack(per_tap, axis=1)
    all_axes = ("sec", "seq", "trk")
    device_count = lax.axis_size(all_axes)
    sq_parts = lax.all_to_all(
        jnp.broadcast_to(jnp.sum(grad_share * grad_share), (device_count,)), all_axes, 0, 0, tiled=True
    )
    total_sq = jnp.sum(sq_parts)
    entries = width_all * lax.axis_size("trk") * slot_count * lane_count
    factor = jnp.minimum(1.0, grad_clip * lax.rsqrt(total_sq / entries + 1e-06))
    head_grad = (grad_share * factor).reshape(share_rows, 1, slot_count, lane_count)
    return (conv_grad, head_grad)


def solution(mesh):
    return jax.shard_map(
        body,
        mesh=mesh,
        in_specs=(
            P("sec", "seq", None),
            P(),
            P(None, None, "trk"),
            P(None, "trk", None, None),
            P("sec", "seq", "trk", None, None),
            P("trk", None),
            P("sec"),
        ),
        out_specs=(P(("sec", "seq"), None, "trk"), P(("sec", "seq"), "trk", None, None)),
        check_vma=False,
    )
```

```python
import math

import jax
import jax.numpy as jnp
from jax import lax
from jax.sharding import PartitionSpec as P

HTRACKS = 7611
MTRACKS = 2608
DILATION_BINS = 16
HTILES = 60


grad_clip = 0.1


def padded(cells, sides, width):
    for axis, dim in sides:
        count = lax.axis_size(axis)
        ends = count - 1
        head = lax.slice_in_dim(cells, 0, width, axis=dim)
        tail = lax.slice_in_dim(cells, cells.shape[dim] - width, cells.shape[dim], axis=dim)
        cells = jnp.concatenate(
            [
                lax.ppermute(tail, axis, [(i, (i + 1) % count) for i in range(ends)]),
                cells,
                lax.ppermute(head, axis, [((i + 1) % count, i) for i in range(ends)]),
            ],
            axis=dim,
        )
    return cells


def contracted_rows(left, right):
    return lax.dot_general(
        left, right, (((0,), (0,)), ((), ())), preferred_element_type=jnp.float32
    )


def ring_scatter(partial):
    rows_all, cols = partial.shape
    sec_n = lax.axis_size("sec")
    x_n = lax.axis_size("seq") // 2
    share = rows_all // (sec_n * x_n * 2)
    sec_i = lax.axis_index("sec")
    x_i = lax.axis_index("seq") // 2
    core_i = lax.axis_index("seq") % 2
    blocks = partial.reshape(sec_n, x_n, 2, share, cols)
    keep = lax.dynamic_index_in_dim(blocks, core_i, 2, keepdims=False)
    give = lax.dynamic_index_in_dim(blocks, 1 - core_i, 2, keepdims=False)
    core_pairs = [(2 * i + j, 2 * i + 1 - j) for i in range(x_n) for j in range(2)]
    summed = keep + lax.ppermute(give, "seq", core_pairs)
    half = cols // 2
    ahead = summed[..., :half]
    behind = summed[..., half:]
    to_next = [(2 * i + j, 2 * ((i + 1) % x_n) + j) for i in range(x_n) for j in range(2)]
    to_prev = [(2 * i + j, 2 * ((i - 1) % x_n) + j) for i in range(x_n) for j in range(2)]
    send_a = lax.dynamic_index_in_dim(ahead, (x_i - 1) % x_n, 1, keepdims=False)
    send_b = lax.dynamic_index_in_dim(behind, (x_i + 1) % x_n, 1, keepdims=False)
    for step in range(x_n - 1):
        got_a = lax.ppermute(send_a, "seq", to_next)
        got_b = lax.ppermute(send_b, "seq", to_prev)
        send_a = got_a + lax.dynamic_index_in_dim(ahead, (x_i - step - 2) % x_n, 1, keepdims=False)
        send_b = got_b + lax.dynamic_index_in_dim(behind, (x_i + step + 2) % x_n, 1, keepdims=False)
    reduced = jnp.concatenate([send_a, send_b], axis=-1)
    total = lax.dynamic_index_in_dim(reduced, sec_i, 0, keepdims=False)
    for shift in range(1, sec_n):
        other = lax.dynamic_index_in_dim(reduced, (sec_i - shift) % sec_n, 0, keepdims=False)
        total = total + lax.ppermute(
            other, "sec", [(i, (i - shift) % sec_n) for i in range(sec_n)]
        )
    return total


def butterfly_sum(value):
    for axis in ("seq", "trk", "sec"):
        count = lax.axis_size(axis)
        bit = 1
        while bit < count:
            value = value + lax.ppermute(value, axis, [(i, i ^ bit) for i in range(count)])
            bit *= 2
    return value


def body(tokens, norm_gain, dilated_conv_weight, head_weight, targets, owner_tiles, species):
    sample_count = tokens.shape[0]
    local_rows = tokens.shape[1]
    width_all = tokens.shape[2]
    tap_count = dilated_conv_weight.shape[1]
    out_share = dilated_conv_weight.shape[2]
    slot_count = head_weight.shape[2]
    lane_count = head_weight.shape[3]
    inputs = tokens.astype(jnp.float32)
    mean_sq = jnp.mean(inputs * inputs, axis=-1, keepdims=True)
    normed = inputs * lax.rsqrt(mean_sq + 1e-06) * norm_gain.astype(jnp.float32)
    hidden_state = jax.nn.gelu(normed).astype(jnp.bfloat16)
    padded_input = padded(hidden_state, (("seq", 1),), DILATION_BINS)
    convolution_output = jnp.zeros((sample_count, local_rows, out_share), jnp.float32)
    for kernel_tap_index in range(tap_count):
        convolution_output = convolution_output + jnp.dot(
            padded_input[
                :, kernel_tap_index * DILATION_BINS : kernel_tap_index * DILATION_BINS + local_rows
            ],
            dilated_conv_weight[:, kernel_tap_index, :],
            preferred_element_type=jnp.float32,
        )
    own_cols = lax.dynamic_slice_in_dim(inputs, lax.axis_index("trk") * out_share, out_share, 2)
    mixed_share = (own_cols + convolution_output).astype(jnp.bfloat16)
    trk_n = lax.axis_size("trk")
    mixed_parts = lax.all_to_all(
        jnp.broadcast_to(mixed_share[:, :, None, :], (sample_count, local_rows, trk_n, out_share)),
        "trk",
        2,
        0,
        tiled=False,
    )
    mixed_all = jnp.transpose(mixed_parts, (1, 2, 0, 3)).reshape(sample_count, local_rows, width_all)
    tiles_here = owner_tiles[0]
    is_mouse = tiles_here >= HTILES
    within = jnp.where(is_mouse, tiles_here - HTILES, tiles_here)
    track_limit = jnp.where(is_mouse, MTRACKS, HTRACKS).astype(jnp.int32)
    lane_ids = jnp.arange(lane_count, dtype=jnp.int32)
    lane_mask = (within[:, None] * lane_count + lane_ids[None, :] < track_limit[:, None]).astype(
        jnp.float32
    )
    grad_scale = 1.0 / math.sqrt(
        lax.axis_size("sec") * sample_count * lax.axis_size("seq") * local_rows
    )
    weights_here = head_weight[:, 0].reshape(width_all, slot_count * lane_count)
    flat_mixed = mixed_all.reshape(sample_count * local_rows, width_all)
    logits = jnp.dot(flat_mixed, weights_here, preferred_element_type=jnp.float32)
    target_cols = targets[:, :, 0].reshape(sample_count * local_rows, slot_count * lane_count)
    active = (tiles_here[None, :] >= 0) & (is_mouse[None, :] == (species[:, None] == 1))
    live_mask = active.astype(jnp.float32)[:, :, None] * lane_mask[None, :, :]
    live_rows = jnp.broadcast_to(
        live_mask.reshape(sample_count, 1, slot_count * lane_count),
        (sample_count, local_rows, slot_count * lane_count),
    ).reshape(sample_count * local_rows, slot_count * lane_count)
    delta_f = (
        grad_scale
        * (jax.nn.softplus(logits) - target_cols.astype(jnp.float32))
        * jax.nn.sigmoid(logits)
        * live_rows
    )
    flat_deltas = delta_f.astype(jnp.bfloat16)
    head_partial = contracted_rows(flat_mixed, flat_deltas)
    deltas_for_back, head_partial = lax.optimization_barrier((flat_deltas, head_partial))
    grad_share = ring_scatter(head_partial)
    back_t = jnp.dot(weights_here, deltas_for_back.T, preferred_element_type=jnp.float32)
    back_from_owners = lax.all_to_all(
        back_t.reshape(trk_n, out_share, sample_count * local_rows), "trk", 0, 0, tiled=True
    )
    backward_portion = jnp.sum(back_from_owners, axis=0).astype(jnp.bfloat16)
    group_count = lax.axis_size("sec") * lax.axis_size("seq")
    share_rows = width_all // group_count
    hidden_parts = lax.all_to_all(
        padded_input.reshape(sample_count, local_rows + 2 * DILATION_BINS, group_count, share_rows),
        ("sec", "seq"),
        2,
        0,
        tiled=False,
    )
    back_parts = lax.all_to_all(
        jnp.broadcast_to(backward_portion[None], (group_count,) + backward_portion.shape),
        ("sec", "seq"),
        0,
        0,
        tiled=True,
    )
    per_tap = [
        lax.dot_general(
            hidden_parts[
                :, :, kernel_tap_index * DILATION_BINS : kernel_tap_index * DILATION_BINS + local_rows
            ].reshape(group_count, sample_count * local_rows, share_rows),
            back_parts,
            (((0, 1), (0, 2)), ((), ())),
            preferred_element_type=jnp.float32,
        )
        for kernel_tap_index in range(tap_count)
    ]
    conv_grad = jnp.stack(per_tap, axis=1)
    all_axes = ("sec", "seq", "trk")
    device_count = lax.axis_size(all_axes)
    sq_parts = lax.all_to_all(
        jnp.broadcast_to(jnp.sum(grad_share * grad_share), (device_count,)), all_axes, 0, 0, tiled=True
    )
    total_sq = jnp.sum(sq_parts)
    entries = width_all * lax.axis_size("trk") * slot_count * lane_count
    factor = jnp.minimum(1.0, grad_clip * lax.rsqrt(total_sq / entries + 1e-06))
    head_grad = (grad_share * factor).reshape(share_rows, 1, slot_count, lane_count)
    return (conv_grad, head_grad)


def solution(mesh):
    return jax.shard_map(
        body,
        mesh=mesh,
        in_specs=(
            P("sec", "seq", None),
            P(),
            P(None, None, "trk"),
            P(None, "trk", None, None),
            P("sec", "seq", "trk", None, None),
            P("trk", None),
            P("sec"),
        ),
        out_specs=(P(("sec", "seq"), None, "trk"), P(("sec", "seq"), "trk", None, None)),
        check_vma=False,
    )
```

```python
import math

import jax
import jax.numpy as jnp
from jax import lax
from jax.sharding import PartitionSpec as P

HTRACKS = 7611
MTRACKS = 2608
DILATION_BINS = 16
HTILES = 60


grad_clip = 0.1


def padded(cells, sides, width):
    for axis, dim in sides:
        count = lax.axis_size(axis)
        ends = count - 1
        head = lax.slice_in_dim(cells, 0, width, axis=dim)
        tail = lax.slice_in_dim(cells, cells.shape[dim] - width, cells.shape[dim], axis=dim)
        cells = jnp.concatenate(
            [
                lax.ppermute(tail, axis, [(i, (i + 1) % count) for i in range(ends)]),
                cells,
                lax.ppermute(head, axis, [((i + 1) % count, i) for i in range(ends)]),
            ],
            axis=dim,
        )
    return cells


def contracted_rows(left, right):
    return lax.dot_general(
        left, right, (((0,), (0,)), ((), ())), preferred_element_type=jnp.float32
    )


def ring_scatter(partial):
    rows_all, cols = partial.shape
    sec_n = lax.axis_size("sec")
    x_n = lax.axis_size("seq") // 2
    share = rows_all // (sec_n * x_n * 2)
    sec_i = lax.axis_index("sec")
    x_i = lax.axis_index("seq") // 2
    core_i = lax.axis_index("seq") % 2
    blocks = partial.reshape(sec_n, x_n, 2, share, cols)
    keep = lax.dynamic_index_in_dim(blocks, core_i, 2, keepdims=False)
    give = lax.dynamic_index_in_dim(blocks, 1 - core_i, 2, keepdims=False)
    core_pairs = [(2 * i + j, 2 * i + 1 - j) for i in range(x_n) for j in range(2)]
    summed = keep + lax.ppermute(give, "seq", core_pairs)
    to_next = [(2 * i + j, 2 * ((i + 1) % x_n) + j) for i in range(x_n) for j in range(2)]
    to_prev = [(2 * i + j, 2 * ((i - 1) % x_n) + j) for i in range(x_n) for j in range(2)]

    def x_ring(data, axis):
        quarter = data.shape[-1] // 2
        ahead = data[..., :quarter]
        behind = data[..., quarter:]
        send_a = lax.dynamic_index_in_dim(ahead, (x_i - 1) % x_n, axis, keepdims=False)
        send_b = lax.dynamic_index_in_dim(behind, (x_i + 1) % x_n, axis, keepdims=False)
        for step in range(x_n - 1):
            got_a = lax.ppermute(send_a, "seq", to_next)
            got_b = lax.ppermute(send_b, "seq", to_prev)
            send_a = got_a + lax.dynamic_index_in_dim(
                ahead, (x_i - step - 2) % x_n, axis, keepdims=False
            )
            send_b = got_b + lax.dynamic_index_in_dim(
                behind, (x_i + step + 2) % x_n, axis, keepdims=False
            )
        return jnp.concatenate([send_a, send_b], axis=-1)

    def sec_pair(data):
        total = lax.dynamic_index_in_dim(data, sec_i, 0, keepdims=False)
        for shift in range(1, sec_n):
            other = lax.dynamic_index_in_dim(data, (sec_i - shift) % sec_n, 0, keepdims=False)
            total = total + lax.ppermute(
                other, "sec", [(i, (i - shift) % sec_n) for i in range(sec_n)]
            )
        return total

    half = cols // 2
    first = sec_pair(x_ring(summed[..., :half], 1))
    second = x_ring(sec_pair(summed[..., half:]), 0)
    return jnp.concatenate([first, second], axis=-1)


def butterfly_sum(value):
    for axis in ("seq", "trk", "sec"):
        count = lax.axis_size(axis)
        bit = 1
        while bit < count:
            value = value + lax.ppermute(value, axis, [(i, i ^ bit) for i in range(count)])
            bit *= 2
    return value


def body(tokens, norm_gain, dilated_conv_weight, head_weight, targets, owner_tiles, species):
    sample_count = tokens.shape[0]
    local_rows = tokens.shape[1]
    width_all = tokens.shape[2]
    tap_count = dilated_conv_weight.shape[1]
    out_share = dilated_conv_weight.shape[2]
    slot_count = head_weight.shape[2]
    lane_count = head_weight.shape[3]
    inputs = tokens.astype(jnp.float32)
    mean_sq = jnp.mean(inputs * inputs, axis=-1, keepdims=True)
    normed = inputs * lax.rsqrt(mean_sq + 1e-06) * norm_gain.astype(jnp.float32)
    hidden_state = jax.nn.gelu(normed).astype(jnp.bfloat16)
    padded_input = padded(hidden_state, (("seq", 1),), DILATION_BINS)
    convolution_output = jnp.zeros((sample_count, local_rows, out_share), jnp.float32)
    for kernel_tap_index in range(tap_count):
        convolution_output = convolution_output + jnp.dot(
            padded_input[
                :, kernel_tap_index * DILATION_BINS : kernel_tap_index * DILATION_BINS + local_rows
            ],
            dilated_conv_weight[:, kernel_tap_index, :],
            preferred_element_type=jnp.float32,
        )
    own_cols = lax.dynamic_slice_in_dim(inputs, lax.axis_index("trk") * out_share, out_share, 2)
    mixed_share = (own_cols + convolution_output).astype(jnp.bfloat16)
    trk_n = lax.axis_size("trk")
    mixed_parts = lax.all_to_all(
        jnp.broadcast_to(mixed_share[:, :, None, :], (sample_count, local_rows, trk_n, out_share)),
        "trk",
        2,
        0,
        tiled=False,
    )
    mixed_all = jnp.transpose(mixed_parts, (1, 2, 0, 3)).reshape(sample_count, local_rows, width_all)
    tiles_here = owner_tiles[0]
    is_mouse = tiles_here >= HTILES
    within = jnp.where(is_mouse, tiles_here - HTILES, tiles_here)
    track_limit = jnp.where(is_mouse, MTRACKS, HTRACKS).astype(jnp.int32)
    lane_ids = jnp.arange(lane_count, dtype=jnp.int32)
    lane_mask = (within[:, None] * lane_count + lane_ids[None, :] < track_limit[:, None]).astype(
        jnp.float32
    )
    grad_scale = 1.0 / math.sqrt(
        lax.axis_size("sec") * sample_count * lax.axis_size("seq") * local_rows
    )
    weights_here = head_weight[:, 0].reshape(width_all, slot_count * lane_count)
    flat_mixed = mixed_all.reshape(sample_count * local_rows, width_all)
    logits = jnp.dot(flat_mixed, weights_here, preferred_element_type=jnp.float32)
    target_cols = targets[:, :, 0].reshape(sample_count * local_rows, slot_count * lane_count)
    active = (tiles_here[None, :] >= 0) & (is_mouse[None, :] == (species[:, None] == 1))
    live_mask = active.astype(jnp.float32)[:, :, None] * lane_mask[None, :, :]
    live_rows = jnp.broadcast_to(
        live_mask.reshape(sample_count, 1, slot_count * lane_count),
        (sample_count, local_rows, slot_count * lane_count),
    ).reshape(sample_count * local_rows, slot_count * lane_count)
    delta_f = (
        grad_scale
        * (jax.nn.softplus(logits) - target_cols.astype(jnp.float32))
        * jax.nn.sigmoid(logits)
        * live_rows
    )
    flat_deltas = delta_f.astype(jnp.bfloat16)
    head_partial = contracted_rows(flat_mixed, flat_deltas)
    deltas_for_back, head_partial = lax.optimization_barrier((flat_deltas, head_partial))
    grad_share = ring_scatter(head_partial)
    back_t = jnp.dot(weights_here, deltas_for_back.T, preferred_element_type=jnp.float32)
    back_from_owners = lax.all_to_all(
        back_t.reshape(trk_n, out_share, sample_count * local_rows), "trk", 0, 0, tiled=True
    )
    backward_portion = jnp.sum(back_from_owners, axis=0).astype(jnp.bfloat16)
    group_count = lax.axis_size("sec") * lax.axis_size("seq")
    share_rows = width_all // group_count
    hidden_parts = lax.all_to_all(
        padded_input.reshape(sample_count, local_rows + 2 * DILATION_BINS, group_count, share_rows),
        ("sec", "seq"),
        2,
        0,
        tiled=False,
    )
    back_parts = lax.all_to_all(
        jnp.broadcast_to(backward_portion[None], (group_count,) + backward_portion.shape),
        ("sec", "seq"),
        0,
        0,
        tiled=True,
    )
    per_tap = [
        lax.dot_general(
            hidden_parts[
                :, :, kernel_tap_index * DILATION_BINS : kernel_tap_index * DILATION_BINS + local_rows
            ].reshape(group_count, sample_count * local_rows, share_rows),
            back_parts,
            (((0, 1), (0, 2)), ((), ())),
            preferred_element_type=jnp.float32,
        )
        for kernel_tap_index in range(tap_count)
    ]
    conv_grad = jnp.stack(per_tap, axis=1)
    all_axes = ("sec", "seq", "trk")
    device_count = lax.axis_size(all_axes)
    sq_parts = lax.all_to_all(
        jnp.broadcast_to(jnp.sum(grad_share * grad_share), (device_count,)), all_axes, 0, 0, tiled=True
    )
    total_sq = jnp.sum(sq_parts)
    entries = width_all * lax.axis_size("trk") * slot_count * lane_count
    factor = jnp.minimum(1.0, grad_clip * lax.rsqrt(total_sq / entries + 1e-06))
    head_grad = (grad_share * factor).reshape(share_rows, 1, slot_count, lane_count)
    return (conv_grad, head_grad)


def solution(mesh):
    return jax.shard_map(
        body,
        mesh=mesh,
        in_specs=(
            P("sec", "seq", None),
            P(),
            P(None, None, "trk"),
            P(None, "trk", None, None),
            P("sec", "seq", "trk", None, None),
            P("trk", None),
            P("sec"),
        ),
        out_specs=(P(("sec", "seq"), None, "trk"), P(("sec", "seq"), "trk", None, None)),
        check_vma=False,
    )
```
